512 devices in a mesh: ep: 128 (over y, z, core), tp: 4 (over x).
Axes of the slice: x: 4, y: 8, z: 8, core: 2. Of those that a mesh axis runs over, the one named last changes fastest.
Arguments:
- tokens: bfloat16 [16384, 2048], P('ep'), may hold values from -6 to 6
- expert_ids: int32 [16384, 2], P('ep'), may hold values from 0 to 127, all different within a row; in each aligned block of 128 rows (0 to 127, 128 to 255, ...) at most 4 rows name the same one
- gate_values: float32 [16384, 2], P('ep'), may hold values from 0.2 to 1
- w_gate: bfloat16 [128, 2048, 1408], P('ep', None, 'tp'), may hold values from -0.125 to 0.125
- w_up: bfloat16 [128, 2048, 1408], P('ep', None, 'tp'), may hold values from -0.125 to 0.125
- w_down: bfloat16 [128, 1408, 2048], P('ep', 'tp'), may hold values from -0.15625 to 0.15625
Outputs:
- mixed: bfloat16 [16384, 2048], P('ep', 'tp')
The draws below stay inside these ranges and needn't reach their ends.
Inputs may be any that keep to these rules, and one draw needn't show every extreme that they name: `expert_ids`: the two experts of a row differ. Within the 128 rows of one block, no expert is chosen more than 4 times, and in every draw some expert is chosen exactly 4 times in some block.
All inputs are finite; a program needn't handle non-finite values.
Results may differ from the reference program's by a relative error of at most 0.017.
Values may be sent and summed in bfloat16 or wider, within the bound.
No kernel may reach another device: no remote copies, remote signals or barrier semaphores. Data moves between devices by JAX's collectives and lax.ppermute only.
A program may use at most 64 MiB of HBM per device.

```python
import math
import jax
import jax.numpy as jnp
import numpy as np
from jax import lax

D = 2048
FF = 1408
TOK_DEV = 128
EXPERTS = 128
CAP = 4
TOKENS = 16384
N_EP = 128
N_TP = 4


def levels(own_key, shape, shards, smallest, high):
    factor_of, own = 1.0, jax.random.fold_in(own_key, 6)
    for dim, blocks in shards:
        heights = jnp.exp(jax.random.uniform(jax.random.fold_in(own, dim), (blocks,), jnp.float32, smallest / len(shards), high / len(shards)))
        factor_of = factor_of * jnp.repeat(heights, shape[dim] // blocks).reshape([-1 if axis == dim else 1 for axis in range(len(shape))])
    return factor_of


def deal_out(rng, own, number, rows, number_of, top, bound, slope):
    ranking = jax.random.permutation(rng, number_of)
    heavy_load, ordinary = shares(number_of, rows * top, bound, slope, True), shares(number_of, rows * top, bound, slope, False)
    places = jnp.arange(number_of)

    def named(tallies, rotation):
        used = int((tallies > 0).sum())
        fixed = max(1, used // 4)
        shifted = fixed + (places - fixed + rotation * (used - fixed)) % max(1, number_of - fixed)
        return jnp.zeros((number_of,), jnp.int32).at[ranking[jnp.where(places < fixed, places, shifted)]].set(jnp.asarray(tallies, jnp.int32))

    tallies = jnp.where(number % 4 == 0, named(heavy_load, number // 4), named(ordinary, number - number // 4 - 1))
    mixed = jax.random.permutation(jax.random.fold_in(own, 3), number_of)
    donor, taker = mixed[0:number_of // 2 * 2:2], mixed[1:number_of // 2 * 2:2]
    slack = jnp.minimum(tallies[donor] - 1, bound - tallies[taker]) // 2
    slack = jnp.where((donor == ranking[0]) | (taker == ranking[0]) | (tallies[taker] == 0), 0, jnp.maximum(slack, 0))
    shifted = jax.random.randint(jax.random.fold_in(own, 4), (number_of // 2,), 0, 1 << 20) % (slack + 1)
    tallies = tallies.at[donor].add(-shifted).at[taker].add(shifted)
    items = jnp.searchsorted(jnp.cumsum(tallies), jnp.arange(rows * top), side="right").astype(jnp.int32)
    listing = items.reshape(top, rows).T
    listing = listing[jax.random.permutation(jax.random.fold_in(own, 1), rows)]
    rotation = jax.random.randint(jax.random.fold_in(own, 2), (rows, 1), 0, top)
    return jnp.take_along_axis(listing, (jnp.arange(top)[None, :] + rotation) % top, axis=1)


def shares(count, total, bound, slope, full):
    loads = [(1 << 20) // math.isqrt(rank ** slope) + 1 for rank in range(1, count + 1)]
    largest = bound if full else min(bound, max(-(-total // count), total * loads[0] // sum(loads)))
    least = 1 if total - largest >= count - 1 else 0
    holding, surplus = [largest] + [least] * (count - 1), total - largest - least * (count - 1)
    while surplus > 0:
        candidates = [i for i in range(1, count) if holding[i] < largest] or [i for i in range(1, count) if holding[i] < bound]
        whole, budget = sum([loads[i] for i in candidates]), surplus
        for i in candidates:
            extra = min(bound - holding[i], max(1, budget * loads[i] // whole), surplus)
            holding[i] = holding[i] + extra
            surplus = surplus - extra
    return np.array(holding)


def noise(rng, extent, deviation, bound, shards=(), kind=jnp.bfloat16):
    drawn = jax.random.normal(rng, extent, jnp.float32) * deviation
    if len(shards) > 0:
        drawn = levels(rng, extent, shards, -0.22, 0.18) * drawn
    return jnp.clip(drawn, min=-bound, max=bound).astype(kind)


def setup_inputs(seed: int = 0) -> dict:
    arg_keys = jax.random.split(jax.random.key(seed), 7)
    tokens = noise(arg_keys[0], (TOKENS, D), 1.0, 6.0, ((0, 128),))
    expert_ids_keys = jax.random.split(jax.random.fold_in(arg_keys[1], 1), TOKENS // TOK_DEV)
    expert_ids_turns = jax.random.permutation(jax.random.fold_in(arg_keys[1], 3), TOKENS // TOK_DEV)
    expert_ids = jax.vmap(lambda own, number: deal_out(jax.random.fold_in(arg_keys[1], 2), own, number, TOK_DEV, EXPERTS, 2, CAP, 2))(expert_ids_keys, expert_ids_turns).reshape((TOKENS, 2))
    gate_values = jnp.clip(0.2 + 0.8 * jax.random.uniform(arg_keys[2], (TOKENS, 2), jnp.float32) ** levels(arg_keys[2], (TOKENS, 2), ((0, 128),), -0.2, 0.2), 0.2, 1.0)
    w_gate = noise(arg_keys[3], (EXPERTS, D, FF), D ** -0.5, 0.125, ((0, 128), (2, 4)))
    w_up = noise(arg_keys[4], (EXPERTS, D, FF), D ** -0.5, 0.125, ((0, 128), (2, 4)))
    w_down = noise(arg_keys[5], (EXPERTS, FF, D), FF ** -0.5, 0.15625, ((0, 128), (1, 4)))
    return {"tokens": tokens, "expert_ids": expert_ids, "gate_values": gate_values, "w_gate": w_gate, "w_up": w_up, "w_down": w_down}


def block_positions(block_ids):
    flat_ids = block_ids.reshape(-1)
    onehot = (flat_ids[:, None] == jnp.arange(EXPERTS, dtype=jnp.int32)[None, :]).astype(jnp.int32)
    running = jnp.cumsum(onehot, axis=0)
    position = jnp.sum(running * onehot, axis=1) - 1
    return position.reshape(block_ids.shape).astype(jnp.int32)


def expert_output(packed):
    inbound, gate_w, up_w, down_w = packed
    gate = jnp.dot(inbound, gate_w, preferred_element_type=jnp.float32)
    up = jnp.dot(inbound, up_w, preferred_element_type=jnp.float32)
    hidden = (jax.nn.silu(gate) * up).astype(jnp.bfloat16)
    group = FF // N_TP
    hidden_g = hidden.reshape(hidden.shape[0], N_TP, group).astype(jnp.float32)
    down_g = down_w.reshape(N_TP, group, D).astype(jnp.float32)
    parts = jnp.einsum("rqf,qfd->qrd", hidden_g, down_g, precision=lax.Precision.HIGHEST)
    parts = parts.astype(jnp.bfloat16)
    return jnp.sum(parts.astype(jnp.float32), axis=0)


def reference(tokens, expert_ids, gate_values, w_gate, w_up, w_down):
    inbound_rows = N_EP * CAP
    block_ids = expert_ids.reshape(N_EP, TOK_DEV, 2)
    position = jax.vmap(block_positions)(block_ids)
    source = jnp.arange(N_EP, dtype=jnp.int32)[:, None, None]
    where = block_ids * inbound_rows + source * CAP + position
    copies = jnp.broadcast_to(tokens.reshape(N_EP, TOK_DEV, 1, D), (N_EP, TOK_DEV, 2, D)).reshape(-1, D)
    buffer = jnp.zeros((EXPERTS * inbound_rows, D), jnp.bfloat16).at[where.reshape(-1)].set(copies)
    buffer = buffer.reshape(EXPERTS, inbound_rows, D)
    outputs = lax.map(expert_output, (buffer, w_gate, w_up, w_down))
    outputs = outputs.reshape(EXPERTS * inbound_rows, D)
    picked = outputs[where.reshape(-1)].reshape(N_EP, TOK_DEV, 2, D)
    weights = gate_values.reshape(N_EP, TOK_DEV, 2, 1)
    mixed = jnp.sum(picked * weights, axis=2)
    return mixed.reshape(TOKENS, D).astype(jnp.bfloat16)
```

```python
import jax
import jax.numpy as jnp
from jax import lax
from jax.sharding import PartitionSpec as P


def shards(tokens, expert_ids, gate_values, w_gate, w_up, w_down):
    tok_rows = tokens.shape[0]
    width = tokens.shape[1]
    experts = lax.axis_size("ep")
    groups = lax.axis_size("tp")
    quarter = width // groups
    capacity = 4 * tok_rows // experts
    row_count = experts * capacity
    flat_ids = expert_ids.reshape(-1)
    onehot = (flat_ids[:, None] == jnp.arange(experts, dtype=jnp.int32)[None, :]).astype(jnp.int32)
    running = jnp.cumsum(onehot, axis=0)
    position = jnp.sum(running * onehot, axis=1) - 1
    target = (flat_ids * capacity + position).reshape(tok_rows, 2)
    slot_iota = jnp.arange(row_count, dtype=jnp.int32)
    first_hit = target[:, 0][None, :] == slot_iota[:, None]
    second_hit = target[:, 1][None, :] == slot_iota[:, None]
    placer = (first_hit | second_hit).astype(jnp.bfloat16)
    outbound = jnp.dot(placer, tokens, preferred_element_type=jnp.float32).astype(jnp.bfloat16)
    arrived = lax.all_to_all(
        outbound.reshape(experts, capacity, width), "ep", split_axis=0, concat_axis=0, tiled=True
    )
    arrived = arrived.reshape(row_count, width)
    gate = jnp.dot(arrived, w_gate[0], preferred_element_type=jnp.float32)
    up = jnp.dot(arrived, w_up[0], preferred_element_type=jnp.float32)
    hidden = (jax.nn.silu(gate) * up).astype(jnp.bfloat16)
    down_q = w_down[0].reshape(w_down.shape[1], groups, quarter)
    partial_out = jnp.einsum(
        "rf,fqd->qrd", hidden, down_q, preferred_element_type=jnp.float32
    ).astype(jnp.bfloat16)
    gathered = lax.all_to_all(partial_out, "tp", split_axis=0, concat_axis=0, tiled=True)
    summed = jnp.sum(gathered.astype(jnp.float32), axis=0).astype(jnp.bfloat16)
    returned = lax.all_to_all(
        summed.reshape(experts, capacity, quarter), "ep", split_axis=0, concat_axis=0, tiled=True
    )
    returned = returned.reshape(row_count, quarter).astype(jnp.float32)
    combine_w = gate_values[:, 0][:, None] * (target[:, 0][:, None] == slot_iota[None, :]).astype(
        jnp.float32
    )
    combine_w = combine_w + gate_values[:, 1][:, None] * (
        target[:, 1][:, None] == slot_iota[None, :]
    ).astype(jnp.float32)
    mixed = jnp.dot(combine_w, returned, precision=lax.Precision.HIGHEST)
    return mixed.astype(jnp.bfloat16)


def solution(mesh):
    placed = (
        P("ep", None),
        P("ep", None),
        P("ep", None),
        P("ep", None, "tp"),
        P("ep", None, "tp"),
        P("ep", "tp", None),
    )
    return jax.shard_map(
        shards, mesh=mesh, in_specs=placed, out_specs=P("ep", "tp"), check_vma=False
    )
```

```python
import jax
import jax.numpy as jnp
from jax import lax
from jax.sharding import PartitionSpec as P


def ring_reduce_scatter(quarter_of, groups, rows):
    half = rows // 2
    up = [(i, (i + 1) % groups) for i in range(groups)]
    down = [(i, (i - 1) % groups) for i in range(groups)]
    carry_a = None
    carry_b = None
    for step in range(1, groups):
        own_a = quarter_of(groups - step, 0, half)
        own_b = quarter_of(step, half, rows)
        send_a = own_a if carry_a is None else own_a + carry_a.astype(jnp.float32)
        send_b = own_b if carry_b is None else own_b + carry_b.astype(jnp.float32)
        carry_a = lax.ppermute(send_a.astype(jnp.bfloat16), "tp", up)
        carry_b = lax.ppermute(send_b.astype(jnp.bfloat16), "tp", down)
    res_a = quarter_of(0, 0, half) + carry_a.astype(jnp.float32)
    res_b = quarter_of(0, half, rows) + carry_b.astype(jnp.float32)
    return jnp.concatenate([res_a, res_b], axis=0)


def shards(tokens, expert_ids, gate_values, w_gate, w_up, w_down):
    tok_rows = tokens.shape[0]
    width = tokens.shape[1]
    experts = lax.axis_size("ep")
    groups = lax.axis_size("tp")
    quarter = width // groups
    capacity = 4 * tok_rows // experts
    row_count = experts * capacity
    flat_ids = expert_ids.reshape(-1)
    onehot = (flat_ids[:, None] == jnp.arange(experts, dtype=jnp.int32)[None, :]).astype(jnp.int32)
    running = jnp.cumsum(onehot, axis=0)
    position = jnp.sum(running * onehot, axis=1) - 1
    target = (flat_ids * capacity + position).reshape(tok_rows, 2)
    slot_iota = jnp.arange(row_count, dtype=jnp.int32)
    first_hit = target[:, 0][None, :] == slot_iota[:, None]
    second_hit = target[:, 1][None, :] == slot_iota[:, None]
    placer = (first_hit | second_hit).astype(jnp.bfloat16)
    outbound = jnp.dot(placer, tokens, preferred_element_type=jnp.float32).astype(jnp.bfloat16)
    arrived = lax.all_to_all(
        outbound.reshape(experts, capacity, width), "ep", split_axis=0, concat_axis=0, tiled=True
    )
    arrived = arrived.reshape(row_count, width)
    gate = jnp.dot(arrived, w_gate[0], preferred_element_type=jnp.float32)
    up = jnp.dot(arrived, w_up[0], preferred_element_type=jnp.float32)
    hidden = (jax.nn.silu(gate) * up).astype(jnp.bfloat16)
    down = w_down[0]
    own = lax.axis_index("tp")

    def quarter_of(k, lo, hi):
        cols = lax.dynamic_slice_in_dim(down, ((own + k) % groups) * quarter, quarter, axis=1)
        part = jnp.dot(hidden[lo:hi], cols, preferred_element_type=jnp.float32)
        return part.astype(jnp.bfloat16).astype(jnp.float32)

    summed = ring_reduce_scatter(quarter_of, groups, row_count).astype(jnp.bfloat16)
    returned = lax.all_to_all(
        summed.reshape(experts, capacity, quarter), "ep", split_axis=0, concat_axis=0, tiled=True
    )
    returned = returned.reshape(row_count, quarter).astype(jnp.float32)
    combine_w = gate_values[:, 0][:, None] * (target[:, 0][:, None] == slot_iota[None, :]).astype(
        jnp.float32
    )
    combine_w = combine_w + gate_values[:, 1][:, None] * (
        target[:, 1][:, None] == slot_iota[None, :]
    ).astype(jnp.float32)
    mixed = jnp.dot(combine_w, returned, precision=lax.Precision.HIGHEST)
    return mixed.astype(jnp.bfloat16)


def solution(mesh):
    placed = (
        P("ep", None),
        P("ep", None),
        P("ep", None),
        P("ep", None, "tp"),
        P("ep", None, "tp"),
        P("ep", "tp", None),
    )
    return jax.shard_map(
        shards, mesh=mesh, in_specs=placed, out_specs=P("ep", "tp"), check_vma=False
    )
```

```python
import jax
import jax.numpy as jnp
from jax import lax
from jax.sharding import PartitionSpec as P


def ring_reduce_scatter(quarter_of, groups, rows):
    half = rows // 2
    up = [(i, (i + 1) % groups) for i in range(groups)]
    down = [(i, (i - 1) % groups) for i in range(groups)]
    far_a = lax.ppermute(quarter_of(2, 0, half).astype(jnp.bfloat16), "tp", up)
    far_b = lax.ppermute(quarter_of(2, half, rows).astype(jnp.bfloat16), "tp", down)
    next_up = quarter_of(1, 0, rows)
    next_up = next_up.at[:half].add(far_a.astype(jnp.float32))
    prev_dn = quarter_of(groups - 1, 0, rows)
    prev_dn = prev_dn.at[half:].add(far_b.astype(jnp.float32))
    from_lo = lax.ppermute(next_up.astype(jnp.bfloat16), "tp", up)
    from_hi = lax.ppermute(prev_dn.astype(jnp.bfloat16), "tp", down)
    return quarter_of(0, 0, rows) + from_lo.astype(jnp.float32) + from_hi.astype(jnp.float32)


def shards(tokens, expert_ids, gate_values, w_gate, w_up, w_down):
    tok_rows = tokens.shape[0]
    width = tokens.shape[1]
    experts = lax.axis_size("ep")
    groups = lax.axis_size("tp")
    quarter = width // groups
    capacity = 4 * tok_rows // experts
    row_count = experts * capacity
    flat_ids = expert_ids.reshape(-1)
    onehot = (flat_ids[:, None] == jnp.arange(experts, dtype=jnp.int32)[None, :]).astype(jnp.int32)
    running = jnp.cumsum(onehot, axis=0)
    position = jnp.sum(running * onehot, axis=1) - 1
    target = (flat_ids * capacity + position).reshape(tok_rows, 2)
    slot_iota = jnp.arange(row_count, dtype=jnp.int32)
    first_hit = target[:, 0][None, :] == slot_iota[:, None]
    second_hit = target[:, 1][None, :] == slot_iota[:, None]
    placer = (first_hit | second_hit).astype(jnp.bfloat16)
    outbound = jnp.dot(placer, tokens, preferred_element_type=jnp.float32).astype(jnp.bfloat16)
    arrived = lax.all_to_all(
        outbound.reshape(experts, capacity, width), "ep", split_axis=0, concat_axis=0, tiled=True
    )
    arrived = arrived.reshape(row_count, width)
    gate = jnp.dot(arrived, w_gate[0], preferred_element_type=jnp.float32)
    up = jnp.dot(arrived, w_up[0], preferred_element_type=jnp.float32)
    hidden = (jax.nn.silu(gate) * up).astype(jnp.bfloat16)
    down = w_down[0]
    own = lax.axis_index("tp")

    def quarter_of(k, lo, hi):
        cols = lax.dynamic_slice_in_dim(down, ((own + k) % groups) * quarter, quarter, axis=1)
        part = jnp.dot(hidden[lo:hi], cols, preferred_element_type=jnp.float32)
        return part.astype(jnp.bfloat16).astype(jnp.float32)

    summed = ring_reduce_scatter(quarter_of, groups, row_count).astype(jnp.bfloat16)
    returned = lax.all_to_all(
        summed.reshape(experts, capacity, quarter), "ep", split_axis=0, concat_axis=0, tiled=True
    )
    returned = returned.reshape(row_count, quarter).astype(jnp.float32)
    combine_w = gate_values[:, 0][:, None] * (target[:, 0][:, None] == slot_iota[None, :]).astype(
        jnp.float32
    )
    combine_w = combine_w + gate_values[:, 1][:, None] * (
        target[:, 1][:, None] == slot_iota[None, :]
    ).astype(jnp.float32)
    mixed = jnp.dot(combine_w, returned, precision=lax.Precision.HIGHEST)
    return mixed.astype(jnp.bfloat16)


def solution(mesh):
    placed = (
        P("ep", None),
        P("ep", None),
        P("ep", None),
        P("ep", None, "tp"),
        P("ep", None, "tp"),
        P("ep", "tp", None),
    )
    return jax.shard_map(
        shards, mesh=mesh, in_specs=placed, out_specs=P("ep", "tp"), check_vma=False
    )
```

```python
import jax
import jax.numpy as jnp
from jax import lax
from jax.sharding import PartitionSpec as P


def ring_reduce_scatter(quarter_of, groups, rows):
    half = rows // 2
    up = [(i, (i + 1) % groups) for i in range(groups)]
    down = [(i, (i - 1) % groups) for i in range(groups)]
    far_a = lax.ppermute(quarter_of(2, 0, half).astype(jnp.bfloat16), "tp", up)
    far_b = lax.ppermute(quarter_of(2, half, rows).astype(jnp.bfloat16), "tp", down)
    next_up = quarter_of(1, 0, rows)
    next_up = next_up.at[:half].add(far_a.astype(jnp.float32))
    prev_dn = quarter_of(groups - 1, 0, rows)
    prev_dn = prev_dn.at[half:].add(far_b.astype(jnp.float32))
    from_lo = lax.ppermute(next_up.astype(jnp.bfloat16), "tp", up)
    from_hi = lax.ppermute(prev_dn.astype(jnp.bfloat16), "tp", down)
    return quarter_of(0, 0, rows) + from_lo.astype(jnp.float32) + from_hi.astype(jnp.float32)


def ring_all_gather(block, groups, rows):
    half = rows // 2
    up = [(i, (i + 1) % groups) for i in range(groups)]
    down = [(i, (i - 1) % groups) for i in range(groups)]
    from_lo = lax.ppermute(block, "tp", up)
    from_hi = lax.ppermute(block, "tp", down)
    far_a = lax.ppermute(from_lo[:half], "tp", up)
    far_b = lax.ppermute(from_hi[half:], "tp", down)
    far = jnp.concatenate([far_a, far_b], axis=0)
    return [(0, block), (groups - 1, from_lo), (1, from_hi), (2, far)]


def shards(tokens, expert_ids, gate_values, w_gate, w_up, w_down):
    tok_rows = tokens.shape[0]
    width = tokens.shape[1]
    experts = lax.axis_size("ep")
    groups = lax.axis_size("tp")
    quarter = width // groups
    capacity = 4 * tok_rows // experts
    row_count = experts * capacity
    flat_ids = expert_ids.reshape(-1)
    onehot = (flat_ids[:, None] == jnp.arange(experts, dtype=jnp.int32)[None, :]).astype(jnp.int32)
    running = jnp.cumsum(onehot, axis=0)
    position = jnp.sum(running * onehot, axis=1) - 1
    target = (flat_ids * capacity + position).reshape(tok_rows, 2)
    slot_iota = jnp.arange(row_count, dtype=jnp.int32)
    first_hit = target[:, 0][None, :] == slot_iota[:, None]
    second_hit = target[:, 1][None, :] == slot_iota[:, None]
    placer = (first_hit | second_hit).astype(jnp.bfloat16)
    own = lax.axis_index("tp")
    own_cols = lax.dynamic_slice_in_dim(tokens, own * quarter, quarter, axis=1)
    outbound = jnp.dot(placer, own_cols, preferred_element_type=jnp.float32).astype(jnp.bfloat16)
    arrived = lax.all_to_all(
        outbound.reshape(experts, capacity, quarter), "ep", split_axis=0, concat_axis=0, tiled=True
    )
    arrived = arrived.reshape(row_count, quarter)
    pieces = ring_all_gather(arrived, groups, row_count)

    def project(weight):
        acc = None
        for k, piece in pieces:
            rows = lax.dynamic_slice_in_dim(weight, ((own + k) % groups) * quarter, quarter, axis=0)
            term = jnp.dot(piece, rows, preferred_element_type=jnp.float32)
            acc = term if acc is None else acc + term
        return acc

    gate = project(w_gate[0])
    up = project(w_up[0])
    hidden = (jax.nn.silu(gate) * up).astype(jnp.bfloat16)
    down = w_down[0]

    def quarter_of(k, lo, hi):
        cols = lax.dynamic_slice_in_dim(down, ((own + k) % groups) * quarter, quarter, axis=1)
        part = jnp.dot(hidden[lo:hi], cols, preferred_element_type=jnp.float32)
        return part.astype(jnp.bfloat16).astype(jnp.float32)

    summed = ring_reduce_scatter(quarter_of, groups, row_count).astype(jnp.bfloat16)
    returned = lax.all_to_all(
        summed.reshape(experts, capacity, quarter), "ep", split_axis=0, concat_axis=0, tiled=True
    )
    returned = returned.reshape(row_count, quarter).astype(jnp.float32)
    combine_w = gate_values[:, 0][:, None] * (target[:, 0][:, None] == slot_iota[None, :]).astype(
        jnp.float32
    )
    combine_w = combine_w + gate_values[:, 1][:, None] * (
        target[:, 1][:, None] == slot_iota[None, :]
    ).astype(jnp.float32)
    mixed = jnp.dot(combine_w, returned, precision=lax.Precision.HIGHEST)
    return mixed.astype(jnp.bfloat16)


def solution(mesh):
    placed = (
        P("ep", None),
        P("ep", None),
        P("ep", None),
        P("ep", None, "tp"),
        P("ep", None, "tp"),
        P("ep", "tp", None),
    )
    return jax.shard_map(
        shards, mesh=mesh, in_specs=placed, out_specs=P("ep", "tp"), check_vma=False
    )
```

```python
import jax
import jax.numpy as jnp
from jax import lax
from jax.sharding import PartitionSpec as P


def shifted(value, groups, shift):
    return lax.ppermute(value, "tp", [(i, (i + shift) % groups) for i in range(groups)])


def ring_reduce_scatter(quarter_of, groups, rows):
    half = rows // 2
    send = lambda k, lo, hi: quarter_of(k, lo, hi).astype(jnp.bfloat16)
    from_lo = shifted(send(1, 0, rows), groups, 1)
    from_hi = shifted(send(groups - 1, 0, rows), groups, -1)
    far_a = shifted(send(2, 0, half), groups, 2)
    far_b = shifted(send(2, half, rows), groups, -2)
    far = jnp.concatenate([far_a, far_b], axis=0).astype(jnp.float32)
    return quarter_of(0, 0, rows) + from_lo.astype(jnp.float32) + from_hi.astype(jnp.float32) + far


def ring_all_gather(block, groups, rows):
    half = rows // 2
    from_lo = shifted(block, groups, 1)
    from_hi = shifted(block, groups, -1)
    far_a = shifted(block[:half], groups, 2)
    far_b = shifted(block[half:], groups, -2)
    far = jnp.concatenate([far_a, far_b], axis=0)
    return [(0, block), (groups - 1, from_lo), (1, from_hi), (2, far)]


def shards(tokens, expert_ids, gate_values, w_gate, w_up, w_down):
    tok_rows = tokens.shape[0]
    width = tokens.shape[1]
    experts = lax.axis_size("ep")
    groups = lax.axis_size("tp")
    quarter = width // groups
    capacity = 4 * tok_rows // experts
    row_count = experts * capacity
    flat_ids = expert_ids.reshape(-1)
    onehot = (flat_ids[:, None] == jnp.arange(experts, dtype=jnp.int32)[None, :]).astype(jnp.int32)
    running = jnp.cumsum(onehot, axis=0)
    position = jnp.sum(running * onehot, axis=1) - 1
    target = (flat_ids * capacity + position).reshape(tok_rows, 2)
    slot_iota = jnp.arange(row_count, dtype=jnp.int32)
    first_hit = target[:, 0][None, :] == slot_iota[:, None]
    second_hit = target[:, 1][None, :] == slot_iota[:, None]
    placer = (first_hit | second_hit).astype(jnp.bfloat16)
    own = lax.axis_index("tp")
    own_cols = lax.dynamic_slice_in_dim(tokens, own * quarter, quarter, axis=1)
    outbound = jnp.dot(placer, own_cols, preferred_element_type=jnp.float32).astype(jnp.bfloat16)
    arrived = lax.all_to_all(
        outbound.reshape(experts, capacity, quarter), "ep", split_axis=0, concat_axis=0, tiled=True
    )
    arrived = arrived.reshape(row_count, quarter)
    pieces = ring_all_gather(arrived, groups, row_count)

    def project(weight):
        acc = None
        for k, piece in pieces:
            rows = lax.dynamic_slice_in_dim(weight, ((own + k) % groups) * quarter, quarter, axis=0)
            term = jnp.dot(piece, rows, preferred_element_type=jnp.float32)
            acc = term if acc is None else acc + term
        return acc

    gate = project(w_gate[0])
    up = project(w_up[0])
    hidden = (jax.nn.silu(gate) * up).astype(jnp.bfloat16)
    down = w_down[0]

    def quarter_of(k, lo, hi):
        cols = lax.dynamic_slice_in_dim(down, ((own + k) % groups) * quarter, quarter, axis=1)
        part = jnp.dot(hidden[lo:hi], cols, preferred_element_type=jnp.float32)
        return part.astype(jnp.bfloat16).astype(jnp.float32)

    summed = ring_reduce_scatter(quarter_of, groups, row_count).astype(jnp.bfloat16)
    returned = lax.all_to_all(
        summed.reshape(experts, capacity, quarter), "ep", split_axis=0, concat_axis=0, tiled=True
    )
    returned = returned.reshape(row_count, quarter).astype(jnp.float32)
    combine_w = gate_values[:, 0][:, None] * (target[:, 0][:, None] == slot_iota[None, :]).astype(
        jnp.float32
    )
    combine_w = combine_w + gate_values[:, 1][:, None] * (
        target[:, 1][:, None] == slot_iota[None, :]
    ).astype(jnp.float32)
    mixed = jnp.dot(combine_w, returned, precision=lax.Precision.HIGHEST)
    return mixed.astype(jnp.bfloat16)


def solution(mesh):
    placed = (
        P("ep", None),
        P("ep", None),
        P("ep", None),
        P("ep", None, "tp"),
        P("ep", None, "tp"),
        P("ep", "tp", None),
    )
    return jax.shard_map(
        shards, mesh=mesh, in_specs=placed, out_specs=P("ep", "tp"), check_vma=False
    )
```

```python
import jax
import jax.numpy as jnp
from jax import lax
from jax.sharding import PartitionSpec as P


def ring_reduce_scatter(quarter_of, groups, rows):
    half = rows // 2
    up = [(i, (i + 1) % groups) for i in range(groups)]
    down = [(i, (i - 1) % groups) for i in range(groups)]
    far_a = lax.ppermute(quarter_of(2, 0, half).astype(jnp.bfloat16), "tp", up)
    far_b = lax.ppermute(quarter_of(2, half, rows).astype(jnp.bfloat16), "tp", down)
    next_up = quarter_of(1, 0, rows)
    next_up = next_up.at[:half].add(far_a.astype(jnp.float32))
    prev_dn = quarter_of(groups - 1, 0, rows)
    prev_dn = prev_dn.at[half:].add(far_b.astype(jnp.float32))
    from_lo = lax.ppermute(next_up.astype(jnp.bfloat16), "tp", up)
    from_hi = lax.ppermute(prev_dn.astype(jnp.bfloat16), "tp", down)
    return quarter_of(0, 0, rows) + from_lo.astype(jnp.float32) + from_hi.astype(jnp.float32)


def ring_all_gather(block, groups, rows):
    half = rows // 2
    up = [(i, (i + 1) % groups) for i in range(groups)]
    down = [(i, (i - 1) % groups) for i in range(groups)]
    from_lo = lax.ppermute(block, "tp", up)
    from_hi = lax.ppermute(block, "tp", down)
    far_a = lax.ppermute(from_lo[:half], "tp", up)
    far_b = lax.ppermute(from_hi[half:], "tp", down)
    far = jnp.concatenate([far_a, far_b], axis=0)
    return [(0, block), (groups - 1, from_lo), (1, from_hi), (2, far)]


def shards(tokens, expert_ids, gate_values, w_gate, w_up, w_down):
    tok_rows = tokens.shape[0]
    width = tokens.shape[1]
    experts = lax.axis_size("ep")
    groups = lax.axis_size("tp")
    quarter = width // groups
    capacity = 4 * tok_rows // experts
    row_count = experts * capacity
    flat_ids = expert_ids.reshape(-1)
    onehot = (flat_ids[:, None] == jnp.arange(experts, dtype=jnp.int32)[None, :]).astype(jnp.int32)
    running = jnp.cumsum(onehot, axis=0)
    position = jnp.sum(running * onehot, axis=1) - 1
    target = (flat_ids * capacity + position).reshape(tok_rows, 2)
    slot_iota = jnp.arange(row_count, dtype=jnp.int32)
    first_hit = target[:, 0][None, :] == slot_iota[:, None]
    second_hit = target[:, 1][None, :] == slot_iota[:, None]
    placer = (first_hit | second_hit).astype(jnp.bfloat16)
    own = lax.axis_index("tp")
    half_cols = width // 2
    side = own % 2
    own_cols = lax.dynamic_slice_in_dim(tokens, side * half_cols, half_cols, axis=1)
    outbound = jnp.dot(placer, own_cols, preferred_element_type=jnp.float32).astype(jnp.bfloat16)
    arrived = lax.all_to_all(
        outbound.reshape(experts, capacity, half_cols), "ep", split_axis=0, concat_axis=0, tiled=True
    )
    arrived = arrived.reshape(row_count, half_cols)
    half_rows = row_count // 2
    other = jnp.concatenate(
        [
            lax.ppermute(arrived[:half_rows], "tp", [(i, (i - 1) % groups) for i in range(groups)]),
            lax.ppermute(arrived[half_rows:], "tp", [(i, (i + 1) % groups) for i in range(groups)]),
        ],
        axis=0,
    )
    pieces = [(side, arrived), (1 - side, other)]

    def project(weight):
        acc = None
        for h, piece in pieces:
            rows = lax.dynamic_slice_in_dim(weight, h * half_cols, half_cols, axis=0)
            term = jnp.dot(piece, rows, preferred_element_type=jnp.float32)
            acc = term if acc is None else acc + term
        return acc

    gate = project(w_gate[0])
    up = project(w_up[0])
    hidden = (jax.nn.silu(gate) * up).astype(jnp.bfloat16)
    down = w_down[0]

    def quarter_of(k, lo, hi):
        cols = lax.dynamic_slice_in_dim(down, ((own + k) % groups) * quarter, quarter, axis=1)
        part = jnp.dot(hidden[lo:hi], cols, preferred_element_type=jnp.float32)
        return part.astype(jnp.bfloat16).astype(jnp.float32)

    summed = ring_reduce_scatter(quarter_of, groups, row_count).astype(jnp.bfloat16)
    returned = lax.all_to_all(
        summed.reshape(experts, capacity, quarter), "ep", split_axis=0, concat_axis=0, tiled=True
    )
    returned = returned.reshape(row_count, quarter).astype(jnp.float32)
    combine_w = gate_values[:, 0][:, None] * (target[:, 0][:, None] == slot_iota[None, :]).astype(
        jnp.float32
    )
    combine_w = combine_w + gate_values[:, 1][:, None] * (
        target[:, 1][:, None] == slot_iota[None, :]
    ).astype(jnp.float32)
    mixed = jnp.dot(combine_w, returned, precision=lax.Precision.HIGHEST)
    return mixed.astype(jnp.bfloat16)


def solution(mesh):
    placed = (
        P("ep", None),
        P("ep", None),
        P("ep", None),
        P("ep", None, "tp"),
        P("ep", None, "tp"),
        P("ep", "tp", None),
    )
    return jax.shard_map(
        shards, mesh=mesh, in_specs=placed, out_specs=P("ep", "tp"), check_vma=False
    )
```

```python
import jax
import jax.numpy as jnp
from jax import lax
from jax.sharding import PartitionSpec as P


def ring_reduce_scatter(quarter_of, groups, rows):
    half = rows // 2
    up = [(i, (i + 1) % groups) for i in range(groups)]
    down = [(i, (i - 1) % groups) for i in range(groups)]
    far_a = lax.ppermute(quarter_of(2, 0, half).astype(jnp.bfloat16), "tp", up)
    far_b = lax.ppermute(quarter_of(2, half, rows).astype(jnp.bfloat16), "tp", down)
    next_up = quarter_of(1, 0, rows)
    next_up = next_up.at[:half].add(far_a.astype(jnp.float32))
    prev_dn = quarter_of(groups - 1, 0, rows)
    prev_dn = prev_dn.at[half:].add(far_b.astype(jnp.float32))
    from_lo = lax.ppermute(next_up.astype(jnp.bfloat16), "tp", up)
    from_hi = lax.ppermute(prev_dn.astype(jnp.bfloat16), "tp", down)
    return quarter_of(0, 0, rows) + from_lo.astype(jnp.float32) + from_hi.astype(jnp.float32)


def ring_all_gather(block, groups, rows):
    half = rows // 2
    up = [(i, (i + 1) % groups) for i in range(groups)]
    down = [(i, (i - 1) % groups) for i in range(groups)]
    from_lo = lax.ppermute(block, "tp", up)
    from_hi = lax.ppermute(block, "tp", down)
    far_a = lax.ppermute(from_lo[:half], "tp", up)
    far_b = lax.ppermute(from_hi[half:], "tp", down)
    return block, from_lo, from_hi, far_a, far_b


def shards(tokens, expert_ids, gate_values, w_gate, w_up, w_down):
    tok_rows = tokens.shape[0]
    width = tokens.shape[1]
    experts = lax.axis_size("ep")
    groups = lax.axis_size("tp")
    quarter = width // groups
    capacity = 4 * tok_rows // experts
    row_count = experts * capacity
    flat_ids = expert_ids.reshape(-1)
    pair_iota = jnp.arange(flat_ids.shape[0], dtype=jnp.int32)
    earlier_same = (flat_ids[:, None] == flat_ids[None, :]) & (pair_iota[None, :] < pair_iota[:, None])
    position = jnp.sum(earlier_same.astype(jnp.int32), axis=1)
    target = (flat_ids * capacity + position).reshape(tok_rows, 2)
    slot_iota = jnp.arange(row_count, dtype=jnp.int32)
    first_hit = target[:, 0][None, :] == slot_iota[:, None]
    second_hit = target[:, 1][None, :] == slot_iota[:, None]
    placer = (first_hit | second_hit).astype(jnp.bfloat16)
    own = lax.axis_index("tp")
    own_cols = lax.dynamic_slice_in_dim(tokens, own * quarter, quarter, axis=1)
    outbound = jnp.dot(placer, own_cols, preferred_element_type=jnp.float32).astype(jnp.bfloat16)
    arrived = lax.all_to_all(
        outbound.reshape(experts, capacity, quarter), "ep", split_axis=0, concat_axis=0, tiled=True
    )
    arrived = arrived.reshape(row_count, quarter)
    block, from_lo, from_hi, far_a, far_b = ring_all_gather(arrived, groups, row_count)
    half = row_count // 2

    def project(weight, lo, hi, far):
        acc = None
        for k, piece in ((0, block[lo:hi]), (groups - 1, from_lo[lo:hi]), (1, from_hi[lo:hi]), (2, far)):
            rows = lax.dynamic_slice_in_dim(weight, ((own + k) % groups) * quarter, quarter, axis=0)
            term = jnp.dot(piece, rows, preferred_element_type=jnp.float32)
            acc = term if acc is None else acc + term
        return acc

    hidden = jnp.concatenate(
        [
            (
                jax.nn.silu(project(w_gate[0], lo, hi, far)) * project(w_up[0], lo, hi, far)
            ).astype(jnp.bfloat16)
            for lo, hi, far in ((0, half, far_a), (half, row_count, far_b))
        ],
        axis=0,
    )
    down = w_down[0]

    def quarter_of(k, lo, hi):
        cols = lax.dynamic_slice_in_dim(down, ((own + k) % groups) * quarter, quarter, axis=1)
        part = jnp.dot(hidden[lo:hi], cols, preferred_element_type=jnp.float32)
        return part.astype(jnp.bfloat16).astype(jnp.float32)

    summed = ring_reduce_scatter(quarter_of, groups, row_count).astype(jnp.bfloat16)
    returned = lax.all_to_all(
        summed.reshape(experts, capacity, quarter), "ep", split_axis=0, concat_axis=0, tiled=True
    )
    returned = returned.reshape(row_count, quarter).astype(jnp.float32)
    combine_w = gate_values[:, 0][:, None] * (target[:, 0][:, None] == slot_iota[None, :]).astype(
        jnp.float32
    )
    combine_w = combine_w + gate_values[:, 1][:, None] * (
        target[:, 1][:, None] == slot_iota[None, :]
    ).astype(jnp.float32)
    mixed = jnp.dot(combine_w, returned, precision=lax.Precision.HIGHEST)
    return mixed.astype(jnp.bfloat16)


def solution(mesh):
    placed = (
        P("ep", None),
        P("ep", None),
        P("ep", None),
        P("ep", None, "tp"),
        P("ep", None, "tp"),
        P("ep", "tp", None),
    )
    return jax.shard_map(
        shards, mesh=mesh, in_specs=placed, out_specs=P("ep", "tp"), check_vma=False
    )
```

```python
import jax
import jax.numpy as jnp
from jax import lax
from jax.sharding import PartitionSpec as P


def ring_reduce_scatter(quarter_of, groups, rows):
    up = [(i, (i + 1) % groups) for i in range(groups)]
    down = [(i, (i - 1) % groups) for i in range(groups)]
    far = lax.ppermute(quarter_of(2, 0, rows).astype(jnp.bfloat16), "tp", up)
    next_up = quarter_of(1, 0, rows) + far.astype(jnp.float32)
    from_lo = lax.ppermute(next_up.astype(jnp.bfloat16), "tp", up)
    from_hi = lax.ppermute(quarter_of(groups - 1, 0, rows).astype(jnp.bfloat16), "tp", down)
    return quarter_of(0, 0, rows) + from_lo.astype(jnp.float32) + from_hi.astype(jnp.float32)


def ring_all_gather(block, groups, rows):
    up = [(i, (i + 1) % groups) for i in range(groups)]
    down = [(i, (i - 1) % groups) for i in range(groups)]
    from_lo = lax.ppermute(block, "tp", up)
    from_hi = lax.ppermute(block, "tp", down)
    far = lax.ppermute(from_lo, "tp", up)
    return [(0, block), (groups - 1, from_lo), (1, from_hi), (2, far)]


def shards(tokens, expert_ids, gate_values, w_gate, w_up, w_down):
    tok_rows = tokens.shape[0]
    width = tokens.shape[1]
    experts = lax.axis_size("ep")
    groups = lax.axis_size("tp")
    quarter = width // groups
    capacity = 4 * tok_rows // experts
    row_count = experts * capacity
    flat_ids = expert_ids.reshape(-1)
    onehot = (flat_ids[:, None] == jnp.arange(experts, dtype=jnp.int32)[None, :]).astype(jnp.int32)
    running = jnp.cumsum(onehot, axis=0)
    position = jnp.sum(running * onehot, axis=1) - 1
    target = (flat_ids * capacity + position).reshape(tok_rows, 2)
    slot_iota = jnp.arange(row_count, dtype=jnp.int32)
    first_hit = target[:, 0][None, :] == slot_iota[:, None]
    second_hit = target[:, 1][None, :] == slot_iota[:, None]
    placer = (first_hit | second_hit).astype(jnp.bfloat16)
    own = lax.axis_index("tp")
    own_cols = lax.dynamic_slice_in_dim(tokens, own * quarter, quarter, axis=1)
    outbound = jnp.dot(placer, own_cols, preferred_element_type=jnp.float32).astype(jnp.bfloat16)
    arrived = lax.all_to_all(
        outbound.reshape(experts, capacity, quarter), "ep", split_axis=0, concat_axis=0, tiled=True
    )
    arrived = arrived.reshape(row_count, quarter)
    pieces = ring_all_gather(arrived, groups, row_count)

    def project(weight):
        acc = None
        for k, piece in pieces:
            rows = lax.dynamic_slice_in_dim(weight, ((own + k) % groups) * quarter, quarter, axis=0)
            term = jnp.dot(piece, rows, preferred_element_type=jnp.float32)
            acc = term if acc is None else acc + term
        return acc

    gate = project(w_gate[0])
    up = project(w_up[0])
    hidden = (jax.nn.silu(gate) * up).astype(jnp.bfloat16)
    down = w_down[0]

    def quarter_of(k, lo, hi):
        cols = lax.dynamic_slice_in_dim(down, ((own + k) % groups) * quarter, quarter, axis=1)
        part = jnp.dot(hidden[lo:hi], cols, preferred_element_type=jnp.float32)
        return part.astype(jnp.bfloat16).astype(jnp.float32)

    summed = ring_reduce_scatter(quarter_of, groups, row_count).astype(jnp.bfloat16)
    returned = lax.all_to_all(
        summed.reshape(experts, capacity, quarter), "ep", split_axis=0, concat_axis=0, tiled=True
    )
    returned = returned.reshape(row_count, quarter).astype(jnp.float32)
    combine_w = gate_values[:, 0][:, None] * (target[:, 0][:, None] == slot_iota[None, :]).astype(
        jnp.float32
    )
    combine_w = combine_w + gate_values[:, 1][:, None] * (
        target[:, 1][:, None] == slot_iota[None, :]
    ).astype(jnp.float32)
    mixed = jnp.dot(combine_w, returned, precision=lax.Precision.HIGHEST)
    return mixed.astype(jnp.bfloat16)


def solution(mesh):
    placed = (
        P("ep", None),
        P("ep", None),
        P("ep", None),
        P("ep", None, "tp"),
        P("ep", None, "tp"),
        P("ep", "tp", None),
    )
    return jax.shard_map(
        shards, mesh=mesh, in_specs=placed, out_specs=P("ep", "tp"), check_vma=False
    )
```

```python
import jax
import jax.numpy as jnp
from jax import lax
from jax.sharding import PartitionSpec as P


def ring_reduce_scatter(quarter_of, groups, rows):
    half = rows // 2
    up = [(i, (i + 1) % groups) for i in range(groups)]
    down = [(i, (i - 1) % groups) for i in range(groups)]
    far_a = lax.ppermute(quarter_of(2, 0, half).astype(jnp.bfloat16), "tp", up)
    far_b = lax.ppermute(quarter_of(2, half, rows).astype(jnp.bfloat16), "tp", down)
    next_up = quarter_of(1, 0, rows)
    next_up = next_up.at[:half].add(far_a.astype(jnp.float32))
    prev_dn = quarter_of(groups - 1, 0, rows)
    prev_dn = prev_dn.at[half:].add(far_b.astype(jnp.float32))
    from_lo = lax.ppermute(next_up.astype(jnp.bfloat16), "tp", up)
    from_hi = lax.ppermute(prev_dn.astype(jnp.bfloat16), "tp", down)
    return quarter_of(0, 0, rows) + from_lo.astype(jnp.float32) + from_hi.astype(jnp.float32)


def ring_all_gather(block, groups, rows):
    half = rows // 2
    up = [(i, (i + 1) % groups) for i in range(groups)]
    down = [(i, (i - 1) % groups) for i in range(groups)]
    from_lo = lax.ppermute(block, "tp", up)
    from_hi = lax.ppermute(block, "tp", down)
    far_a = lax.ppermute(from_lo[:half], "tp", up)
    far_b = lax.ppermute(from_hi[half:], "tp", down)
    far = jnp.concatenate([far_a, far_b], axis=0)
    return [(0, block), (groups - 1, from_lo), (1, from_hi), (2, far)]


def shards(tokens, expert_ids, gate_values, w_gate, w_up, w_down):
    tok_rows = tokens.shape[0]
    width = tokens.shape[1]
    experts = lax.axis_size("ep")
    groups = lax.axis_size("tp")
    quarter = width // groups
    capacity = 4 * tok_rows // experts
    row_count = experts * capacity
    flat_ids = expert_ids.reshape(-1)
    onehot = (flat_ids[:, None] == jnp.arange(experts, dtype=jnp.int32)[None, :]).astype(jnp.int32)
    running = jnp.cumsum(onehot, axis=0)
    position = jnp.sum(running * onehot, axis=1) - 1
    target = (flat_ids * capacity + position).reshape(tok_rows, 2)
    slot_iota = jnp.arange(row_count, dtype=jnp.int32)
    first_hit = target[:, 0][None, :] == slot_iota[:, None]
    second_hit = target[:, 1][None, :] == slot_iota[:, None]
    placer = (first_hit | second_hit).astype(jnp.bfloat16)
    own = lax.axis_index("tp")
    own_cols = lax.dynamic_slice_in_dim(tokens, own * quarter, quarter, axis=1)
    outbound = jnp.dot(placer, own_cols, preferred_element_type=jnp.float32).astype(jnp.bfloat16)
    arrived = lax.all_to_all(
        outbound.reshape(experts, capacity, quarter), "ep", split_axis=0, concat_axis=0, tiled=True
    )
    arrived = arrived.reshape(row_count, quarter)
    pieces = ring_all_gather(arrived, groups, row_count)

    def project(weight):
        acc = None
        for k, piece in pieces:
            rows = lax.dynamic_slice_in_dim(weight, ((own + k) % groups) * quarter, quarter, axis=0)
            term = jnp.dot(piece, rows, preferred_element_type=jnp.float32)
            acc = term if acc is None else acc + term
        return acc

    gate = project(w_gate[0])
    up = project(w_up[0])
    hidden = (jax.nn.silu(gate) * up).astype(jnp.bfloat16)
    down = w_down[0]

    def quarter_of(k, lo, hi):
        cols = lax.dynamic_slice_in_dim(down, ((own + k) % groups) * quarter, quarter, axis=1)
        part = jnp.dot(hidden[lo:hi], cols, preferred_element_type=jnp.float32)
        return part.astype(jnp.bfloat16).astype(jnp.float32)

    summed = ring_reduce_scatter(quarter_of, groups, row_count).astype(jnp.bfloat16)
    returned = lax.all_to_all(
        summed.reshape(experts, capacity, quarter), "ep", split_axis=0, concat_axis=0, tiled=True
    )
    returned = returned.reshape(row_count, quarter)
    mixed = None
    for k in range(2):
        pick = (target[:, k][:, None] == slot_iota[None, :]).astype(jnp.bfloat16)
        chosen = jnp.dot(pick, returned, preferred_element_type=jnp.float32)
        term = gate_values[:, k][:, None] * chosen
        mixed = term if mixed is None else mixed + term
    return mixed.astype(jnp.bfloat16)


def solution(mesh):
    placed = (
        P("ep", None),
        P("ep", None),
        P("ep", None),
        P("ep", None, "tp"),
        P("ep", None, "tp"),
        P("ep", "tp", None),
    )
    return jax.shard_map(
        shards, mesh=mesh, in_specs=placed, out_specs=P("ep", "tp"), check_vma=False
    )
```

```python
import jax
import jax.numpy as jnp
from jax import lax
from jax.sharding import PartitionSpec as P


def ring_reduce_scatter(quarter_of, groups, rows):
    half = rows // 2
    up = [(i, (i + 1) % groups) for i in range(groups)]
    down = [(i, (i - 1) % groups) for i in range(groups)]
    far_a = lax.ppermute(quarter_of(2, 0, half).astype(jnp.bfloat16), "tp", up)
    far_b = lax.ppermute(quarter_of(2, half, rows).astype(jnp.bfloat16), "tp", down)
    next_up = quarter_of(1, 0, rows)
    next_up = next_up.at[:half].add(far_a.astype(jnp.float32))
    prev_dn = quarter_of(groups - 1, 0, rows)
    prev_dn = prev_dn.at[half:].add(far_b.astype(jnp.float32))
    from_lo = lax.ppermute(next_up.astype(jnp.bfloat16), "tp", up)
    from_hi = lax.ppermute(prev_dn.astype(jnp.bfloat16), "tp", down)
    return quarter_of(0, 0, rows) + from_lo.astype(jnp.float32) + from_hi.astype(jnp.float32)


def ring_all_gather(block, groups, rows):
    half = rows // 2
    up = [(i, (i + 1) % groups) for i in range(groups)]
    down = [(i, (i - 1) % groups) for i in range(groups)]
    from_lo = lax.ppermute(block, "tp", up)
    from_hi = lax.ppermute(block, "tp", down)
    far_a = lax.ppermute(from_lo[:half], "tp", up)
    far_b = lax.ppermute(from_hi[half:], "tp", down)
    far = jnp.concatenate([far_a, far_b], axis=0)
    return [(0, block), (groups - 1, from_lo), (1, from_hi), (2, far)]


def shards(tokens, expert_ids, gate_values, w_gate, w_up, w_down):
    tok_rows = tokens.shape[0]
    width = tokens.shape[1]
    experts = lax.axis_size("ep")
    groups = lax.axis_size("tp")
    quarter = width // groups
    capacity = 4 * tok_rows // experts
    row_count = experts * capacity
    row_iota = jnp.arange(tok_rows, dtype=jnp.int32)
    earlier = (row_iota[None, :] < row_iota[:, None]).astype(jnp.int32)
    first, second = expert_ids[:, 0], expert_ids[:, 1]
    same_row = (first == second).astype(jnp.int32)
    targets = []
    for k, ids in enumerate((first, second)):
        hits = (ids[:, None] == first[None, :]).astype(jnp.int32) + (
            ids[:, None] == second[None, :]
        ).astype(jnp.int32)
        position = jnp.sum(hits * earlier, axis=1) + (same_row if k == 1 else 0)
        targets.append(ids * capacity + position)
    target = jnp.stack(targets, axis=1)
    slot_iota = jnp.arange(row_count, dtype=jnp.int32)
    first_hit = target[:, 0][None, :] == slot_iota[:, None]
    second_hit = target[:, 1][None, :] == slot_iota[:, None]
    placer = (first_hit | second_hit).astype(jnp.bfloat16)
    own = lax.axis_index("tp")
    own_cols = lax.dynamic_slice_in_dim(tokens, own * quarter, quarter, axis=1)
    outbound = jnp.dot(placer, own_cols, preferred_element_type=jnp.float32).astype(jnp.bfloat16)
    arrived = lax.all_to_all(
        outbound.reshape(experts, capacity, quarter), "ep", split_axis=0, concat_axis=0, tiled=True
    )
    arrived = arrived.reshape(row_count, quarter)
    pieces = ring_all_gather(arrived, groups, row_count)

    def project(weight):
        acc = None
        for k, piece in pieces:
            rows = lax.dynamic_slice_in_dim(weight, ((own + k) % groups) * quarter, quarter, axis=0)
            term = jnp.dot(piece, rows, preferred_element_type=jnp.float32)
            acc = term if acc is None else acc + term
        return acc

    gate = project(w_gate[0])
    up = project(w_up[0])
    hidden = (jax.nn.silu(gate) * up).astype(jnp.bfloat16)
    down = w_down[0]

    def quarter_of(k, lo, hi):
        cols = lax.dynamic_slice_in_dim(down, ((own + k) % groups) * quarter, quarter, axis=1)
        part = jnp.dot(hidden[lo:hi], cols, preferred_element_type=jnp.float32)
        return part.astype(jnp.bfloat16).astype(jnp.float32)

    summed = ring_reduce_scatter(quarter_of, groups, row_count).astype(jnp.bfloat16)
    returned = lax.all_to_all(
        summed.reshape(experts, capacity, quarter), "ep", split_axis=0, concat_axis=0, tiled=True
    )
    returned = returned.reshape(row_count, quarter)
    mixed = None
    for k in range(2):
        pick = (target[:, k][:, None] == slot_iota[None, :]).astype(jnp.bfloat16)
        chosen = jnp.dot(pick, returned, preferred_element_type=jnp.float32)
        term = gate_values[:, k][:, None] * chosen
        mixed = term if mixed is None else mixed + term
    return mixed.astype(jnp.bfloat16)


def solution(mesh):
    placed = (
        P("ep", None),
        P("ep", None),
        P("ep", None),
        P("ep", None, "tp"),
        P("ep", None, "tp"),
        P("ep", "tp", None),
    )
    return jax.shard_map(
        shards, mesh=mesh, in_specs=placed, out_specs=P("ep", "tp"), check_vma=False
    )
```

```python
import jax
import jax.numpy as jnp
from jax import lax
from jax.sharding import PartitionSpec as P


def ring_reduce_scatter(quarter_of, groups, rows):
    half = rows // 2
    up = [(i, (i + 1) % groups) for i in range(groups)]
    down = [(i, (i - 1) % groups) for i in range(groups)]
    far_a = lax.ppermute(quarter_of(2, 0, half).astype(jnp.bfloat16), "tp", up)
    far_b = lax.ppermute(quarter_of(2, half, rows).astype(jnp.bfloat16), "tp", down)
    next_up = quarter_of(1, 0, rows)
    next_up = next_up.at[:half].add(far_a.astype(jnp.float32))
    prev_dn = quarter_of(groups - 1, 0, rows)
    prev_dn = prev_dn.at[half:].add(far_b.astype(jnp.float32))
    from_lo = lax.ppermute(next_up.astype(jnp.bfloat16), "tp", up)
    from_hi = lax.ppermute(prev_dn.astype(jnp.bfloat16), "tp", down)
    return quarter_of(0, 0, rows) + from_lo.astype(jnp.float32) + from_hi.astype(jnp.float32)


def ring_all_gather(block, groups, rows):
    half = rows // 2
    up = [(i, (i + 1) % groups) for i in range(groups)]
    down = [(i, (i - 1) % groups) for i in range(groups)]
    from_lo = lax.ppermute(block, "tp", up)
    from_hi = lax.ppermute(block, "tp", down)
    far_a = lax.ppermute(from_lo[:half], "tp", up)
    far_b = lax.ppermute(from_hi[half:], "tp", down)
    far = jnp.concatenate([far_a, far_b], axis=0)
    return [(0, block), (groups - 1, from_lo), (1, from_hi), (2, far)]


def shards(tokens, expert_ids, gate_values, w_gate, w_up, w_down):
    tok_rows = tokens.shape[0]
    width = tokens.shape[1]
    experts = lax.axis_size("ep")
    groups = lax.axis_size("tp")
    quarter = width // groups
    capacity = 4 * tok_rows // experts
    row_count = experts * capacity
    row_iota = jnp.arange(tok_rows, dtype=jnp.int32)
    earlier = (row_iota[None, :] < row_iota[:, None]).astype(jnp.int32)
    first, second = expert_ids[:, 0], expert_ids[:, 1]
    same_row = (first == second).astype(jnp.int32)
    targets = []
    for k, ids in enumerate((first, second)):
        hits = (ids[:, None] == first[None, :]).astype(jnp.int32) + (
            ids[:, None] == second[None, :]
        ).astype(jnp.int32)
        position = jnp.sum(hits * earlier, axis=1) + (same_row if k == 1 else 0)
        targets.append(ids * capacity + position)
    target = jnp.stack(targets, axis=1)
    slot_iota = jnp.arange(row_count, dtype=jnp.int32)
    first_hit = target[:, 0][None, :] == slot_iota[:, None]
    second_hit = target[:, 1][None, :] == slot_iota[:, None]
    placer = (first_hit | second_hit).astype(jnp.bfloat16)
    own = lax.axis_index("tp")
    own_cols = lax.dynamic_slice_in_dim(tokens, own * quarter, quarter, axis=1)
    outbound = jnp.dot(placer, own_cols, preferred_element_type=jnp.float32).astype(jnp.bfloat16)
    arrived = lax.all_to_all(
        outbound.reshape(experts, capacity, quarter), "ep", split_axis=0, concat_axis=0, tiled=True
    )
    pieces = [
        (k, piece.reshape(row_count, quarter)) for k, piece in ring_all_gather(arrived, groups, experts)
    ]

    def project(weight):
        acc = None
        for k, piece in pieces:
            rows = lax.dynamic_slice_in_dim(weight, ((own + k) % groups) * quarter, quarter, axis=0)
            term = jnp.dot(piece, rows, preferred_element_type=jnp.float32)
            acc = term if acc is None else acc + term
        return acc

    gate = project(w_gate[0])
    up = project(w_up[0])
    hidden = (jax.nn.silu(gate) * up).astype(jnp.bfloat16)
    down = w_down[0]

    def quarter_of(k, lo, hi):
        cols = lax.dynamic_slice_in_dim(down, ((own + k) % groups) * quarter, quarter, axis=1)
        part = jnp.dot(hidden[lo:hi], cols, preferred_element_type=jnp.float32)
        return part.astype(jnp.bfloat16).astype(jnp.float32)

    summed = ring_reduce_scatter(quarter_of, groups, row_count).astype(jnp.bfloat16)
    returned = lax.all_to_all(
        summed.reshape(experts, capacity, quarter), "ep", split_axis=0, concat_axis=0, tiled=True
    )
    returned = returned.reshape(row_count, quarter)
    mixed = None
    for k in range(2):
        pick = (target[:, k][:, None] == slot_iota[None, :]).astype(jnp.bfloat16)
        chosen = jnp.dot(pick, returned, preferred_element_type=jnp.float32)
        term = gate_values[:, k][:, None] * chosen
        mixed = term if mixed is None else mixed + term
    return mixed.astype(jnp.bfloat16)


def solution(mesh):
    placed = (
        P("ep", None),
        P("ep", None),
        P("ep", None),
        P("ep", None, "tp"),
        P("ep", None, "tp"),
        P("ep", "tp", None),
    )
    return jax.shard_map(
        shards, mesh=mesh, in_specs=placed, out_specs=P("ep", "tp"), check_vma=False
    )
```
